256 devices in a mesh: target: 32 (over x_lo, z, core), surface: 8 (over x_hi, y).
Axes of the slice: x: 4 (x_hi: 2, x_lo: 2; x = x_hi * 2 + x_lo), y: 4, z: 8, core: 2. Of those that a mesh axis runs over, the one named last changes fastest.
Arguments:
- response: float32 [64, 32, 32, 512], P('target', None, 'surface'), may hold values from -6 to 6
- data_spectra: bfloat16 [32, 16, 2, 32, 32, 256], P('target', None, None, 'surface'), may hold values from -0.01171875 to 0.01171875
- observed: bfloat16 [32, 2, 32, 32, 256], P('target', None, None, 'surface'), may hold values from -6 to 6
- block_lists: int32 [32, 16], replicated, may hold values from 0 to 63, as said below
Outputs:
- response_next: float32 [64, 32, 32, 512], P('target', None, 'surface')
- response_copy: bfloat16 [64, 32, 32, 512], P('target', None, 'surface')
- residual: float32 [32, 2, 32, 32, 256], P('target', None, None, 'surface')
The draws below stay inside these ranges and needn't reach their ends.
Inputs may be any that keep to these rules, and one draw needn't show every extreme that they name: `block_lists`: block b is owned by index b // 2 of target. Each tile lists 16 blocks, no two of the same owner.
All inputs are finite; a program needn't handle non-finite values.
Results may differ from the reference program's by a relative error of at most 0.0048.
Values may be sent and summed in bfloat16 or wider, within the bound.
No kernel may reach another device: no remote copies, remote signals or barrier semaphores. Data moves between devices by JAX's collectives and lax.ppermute only.
A program may use at most 128 MiB of HBM per device.

```python
import math
import jax
import jax.numpy as jnp
from jax import lax

SHOT = 32
RECV = 32
TS = 512
F = 256
LIST = 16
R_DEV = 2
TILES = 32
NBLK = 64
SBT = 32


def draw_block_lists(key, part):
    owners = NBLK // R_DEV
    tile_keys = jax.random.split(jax.random.fold_in(key, 11), TILES)

    def one_tile(tile_key):
        return jax.random.permutation(tile_key, owners)[:LIST]
    chosen = jax.vmap(one_tile)(tile_keys)
    slots = jax.random.randint(jax.random.fold_in(key, 12), (TILES, LIST), 0, R_DEV)
    return (chosen * R_DEV + slots).astype(jnp.int32)


def block_scale(rng, dims, pieces, smallest, top_value):
    gain = 1.0
    for axis_at, parts in pieces:
        draws = jax.random.uniform(jax.random.fold_in(jax.random.fold_in(rng, 6), axis_at), (parts,), jnp.float32, smallest / len(pieces), top_value / len(pieces))
        gain = gain * jnp.repeat(jnp.exp(draws), dims[axis_at] // parts).reshape((-1,) + (1,) * (len(dims) - 1 - axis_at))
    return gain


def normal_values(own_key, dims, spread, most, shards=(), dtype=jnp.bfloat16):
    level = block_scale(own_key, dims, shards, -0.22, 0.18) if shards else 1.0
    result = jax.random.normal(own_key, dims, jnp.float32) * spread * level
    return jnp.minimum(jnp.maximum(result, -most), most).astype(dtype)


def setup_inputs(seed: int = 0) -> dict:
    key_list = jax.random.split(jax.random.key(seed), 5)
    response = normal_values(key_list[0], (NBLK, SHOT, SBT, TS), 1.0, 6.0, ((0, 32), (2, 8)), jnp.float32)
    data_spectra = normal_values(key_list[1], (TILES, LIST, 2, SBT, RECV, F), (TS * LIST * SBT) ** -0.5, 0.01171875, ((0, 32), (3, 8)))
    observed = normal_values(key_list[2], (TILES, 2, SHOT, RECV, F), 1.0, 6.0, ((0, 32), (3, 8)))
    block_lists = draw_block_lists(jax.random.fold_in(key_list[4], 71), 0)
    return {"response": response, "data_spectra": data_spectra, "observed": observed, "block_lists": block_lists}


def make_table(samples):
    freqs = samples // 2
    sample_index = lax.broadcasted_iota(jnp.int32, (samples, freqs), 0)
    freq_index = lax.broadcasted_iota(jnp.int32, (samples, freqs), 1)
    phase = ((sample_index * freq_index) % samples).astype(jnp.float32) * (2.0 * math.pi / samples)
    return jnp.concatenate([jnp.cos(phase), -jnp.sin(phase)], axis=1)


def contract(spec, listed):
    return jnp.einsum("lakf,lkrf->arf", spec, listed, precision=lax.Precision.HIGHEST)


def correlate(misfit_part, listed):
    return jnp.einsum("arf,lkrf->lakf", misfit_part, listed, precision=lax.Precision.HIGHEST)


def reference(response, data_spectra, observed, block_lists):
    dft_table = make_table(TS)
    table_half = dft_table.astype(jnp.bfloat16)
    copy_now = response.astype(jnp.bfloat16)
    all_spectra = jnp.dot(copy_now, table_half, preferred_element_type=jnp.float32).astype(jnp.bfloat16)
    freqs = TS // 2

    def per_tile(carry, inputs):
        listed_ids, listed_data, observed_tile = inputs
        spectra = all_spectra[listed_ids].astype(jnp.float32)
        spec_real = spectra[..., :freqs]
        spec_imag = spectra[..., freqs:]
        data_real = listed_data[:, 0].astype(jnp.float32)
        data_imag = listed_data[:, 1].astype(jnp.float32)
        pred_real = contract(spec_real, data_real) - contract(spec_imag, data_imag)
        pred_imag = contract(spec_real, data_imag) + contract(spec_imag, data_real)
        residual_tile = observed_tile.astype(jnp.float32) - jnp.stack([pred_real, pred_imag])
        misfit = lax.optimization_barrier(residual_tile.astype(jnp.bfloat16)).astype(jnp.float32)
        misfit_real = misfit[0]
        misfit_imag = misfit[1]
        grad_real = -(correlate(misfit_real, data_real) + correlate(misfit_imag, data_imag))
        grad_imag = correlate(misfit_real, data_imag) - correlate(misfit_imag, data_real)
        grad_spectra = jnp.concatenate([grad_real, grad_imag], axis=-1)
        carry = carry.at[listed_ids].add(grad_spectra)
        return carry, residual_tile

    start = jnp.zeros(all_spectra.shape, jnp.float32)
    summed, residual = lax.scan(per_tile, start, (block_lists, data_spectra, observed))
    gradient = jnp.dot(summed, dft_table.T, precision=lax.Precision.HIGHEST)
    response_next = response - 0.5 * gradient
    return response_next, response_next.astype(jnp.bfloat16), residual
```

```python
import math

import jax
import jax.numpy as jnp
from jax import lax
from jax.sharding import PartitionSpec as P

step_length = 0.5


def make_table(samples):
    freqs = samples // 2
    sample_index = lax.broadcasted_iota(jnp.int32, (samples, freqs), 0)
    freq_index = lax.broadcasted_iota(jnp.int32, (samples, freqs), 1)
    phase = (sample_index * freq_index % samples).astype(jnp.float32) * (2.0 * math.pi / samples)
    return jnp.concatenate([jnp.cos(phase), -jnp.sin(phase)], axis=1)


def contract(spec, listed):
    return jnp.einsum("lakf,lkrf->arf", spec, listed, preferred_element_type=jnp.float32)


def correlate(misfit_part, listed):
    return jnp.einsum("arf,lkrf->lakf", misfit_part, listed, preferred_element_type=jnp.float32)


def per_device(response, data_spectra, observed, block_lists):
    owners = lax.axis_size("target")
    my_index = lax.axis_index("target")
    owned = response.shape[0]
    samples = response.shape[3]
    freqs = samples // 2
    dft_table = make_table(samples)
    table_half = dft_table.astype(jnp.bfloat16)
    own_ids = lax.dynamic_slice_in_dim(block_lists, my_index, 1, 0)[0]
    own_owner = own_ids // owned
    wanted = block_lists // owned == my_index
    present = jnp.any(wanted, axis=1)
    slot_for = jnp.sum(jnp.where(wanted, block_lists % owned, 0), axis=1)
    picker = (
        (slot_for[None, :] == jnp.arange(owned, dtype=jnp.int32)[:, None]) & present[None, :]
    ).astype(jnp.float32)
    present_rows = present[:, None, None, None]
    zero_half = jnp.zeros((), jnp.bfloat16)
    copy_now = response.astype(jnp.bfloat16)
    outgoing = jnp.where(present_rows, copy_now[slot_for], zero_half)
    arrived = lax.all_to_all(outgoing, "target", split_axis=0, concat_axis=0, tiled=True)
    spectra = jnp.dot(arrived[own_owner], table_half, preferred_element_type=jnp.float32).astype(
        jnp.bfloat16
    )
    listed_data = data_spectra[0]
    spec_real = spectra[..., :freqs]
    spec_imag = spectra[..., freqs:]
    data_real = listed_data[:, 0]
    data_imag = listed_data[:, 1]
    partial_value = jnp.stack(
        [
            contract(spec_real, data_real) - contract(spec_imag, data_imag),
            contract(spec_real, data_imag) + contract(spec_imag, data_real),
        ]
    )
    observed_share = observed[0].astype(jnp.float32)
    summed_share = lax.psum_scatter(partial_value, "surface", scatter_dimension=2, tiled=True)
    residual_share = observed_share - summed_share
    misfit = lax.all_gather(residual_share.astype(jnp.bfloat16), "surface", axis=2, tiled=True)
    misfit_real = misfit[0]
    misfit_imag = misfit[1]
    grad_spectra = jnp.concatenate(
        [
            -(correlate(misfit_real, data_real) + correlate(misfit_imag, data_imag)),
            correlate(misfit_real, data_imag) - correlate(misfit_imag, data_real),
        ],
        axis=-1,
    )
    grad_time = jnp.dot(grad_spectra, dft_table.T, precision=lax.Precision.HIGHEST)
    grad_half = grad_time.astype(jnp.bfloat16)
    returning = jnp.zeros((owners,) + grad_time.shape[1:], jnp.bfloat16).at[own_owner].set(grad_half)
    received = lax.all_to_all(returning, "target", split_axis=0, concat_axis=0, tiled=True)
    flat = received.reshape(owners, -1)
    gradient = jnp.dot(
        picker.astype(jnp.bfloat16), flat, preferred_element_type=jnp.float32
    ).reshape(response.shape)
    response_next = response - step_length * gradient
    return (response_next, response_next.astype(jnp.bfloat16), residual_share[None])


def solution(mesh):
    return jax.shard_map(
        per_device,
        mesh=mesh,
        in_specs=(
            P("target", None, "surface", None),
            P("target", None, None, "surface", None, None),
            P("target", None, None, "surface", None),
            P(),
        ),
        out_specs=(
            P("target", None, "surface", None),
            P("target", None, "surface", None),
            P("target", None, None, "surface", None),
        ),
        check_vma=False,
    )
```

```python
import math

import jax
import jax.numpy as jnp
from jax import lax
from jax.sharding import PartitionSpec as P

step_length = 0.5


def make_table(samples):
    freqs = samples // 2
    sample_index = lax.broadcasted_iota(jnp.int32, (samples, freqs), 0)
    freq_index = lax.broadcasted_iota(jnp.int32, (samples, freqs), 1)
    phase = (sample_index * freq_index % samples).astype(jnp.float32) * (2.0 * math.pi / samples)
    return jnp.concatenate([jnp.cos(phase), -jnp.sin(phase)], axis=1)


def contract(spec, listed):
    return jnp.einsum("lakf,lkrf->arf", spec, listed, preferred_element_type=jnp.float32)


def correlate(misfit_part, listed):
    return jnp.einsum("arf,lkrf->lakf", misfit_part, listed, preferred_element_type=jnp.float32)


def per_device(response, data_spectra, observed, block_lists):
    owners = lax.axis_size("target")
    my_index = lax.axis_index("target")
    owned = response.shape[0]
    samples = response.shape[3]
    freqs = samples // 2
    dft_table = make_table(samples)
    table_half = dft_table.astype(jnp.bfloat16)
    own_ids = lax.dynamic_slice_in_dim(block_lists, my_index, 1, 0)[0]
    own_owner = own_ids // owned
    wanted = block_lists // owned == my_index
    present = jnp.any(wanted, axis=1)
    slot_for = jnp.sum(jnp.where(wanted, block_lists % owned, 0), axis=1)
    picker = (
        (slot_for[None, :] == jnp.arange(owned, dtype=jnp.int32)[:, None]) & present[None, :]
    ).astype(jnp.float32)
    present_rows = present[:, None, None, None]
    zero_half = jnp.zeros((), jnp.bfloat16)
    copy_now = response.astype(jnp.bfloat16)
    outgoing = jnp.where(present_rows, copy_now[slot_for], zero_half)
    arrived = lax.all_to_all(outgoing, "target", split_axis=0, concat_axis=0, tiled=True)
    spectra = jnp.dot(arrived[own_owner], table_half, preferred_element_type=jnp.float32).astype(
        jnp.bfloat16
    )
    listed_data = data_spectra[0]
    spec_real = spectra[..., :freqs]
    spec_imag = spectra[..., freqs:]
    data_real = listed_data[:, 0]
    data_imag = listed_data[:, 1]
    partial_value = jnp.stack(
        [
            contract(spec_real, data_real) - contract(spec_imag, data_imag),
            contract(spec_real, data_imag) + contract(spec_imag, data_real),
        ]
    )
    observed_share = observed[0].astype(jnp.float32)
    channels = lax.axis_size("surface")
    parts, shots, recvs = partial_value.shape[0], partial_value.shape[1], partial_value.shape[2]
    split_value = partial_value.reshape(parts, shots, channels, recvs // channels, freqs)
    exchanged = lax.all_to_all(split_value, "surface", split_axis=2, concat_axis=2, tiled=True)
    summed_share = jnp.sum(exchanged, axis=2)
    residual_share = observed_share - summed_share
    misfit_share = residual_share.astype(jnp.bfloat16)
    spread = jnp.broadcast_to(misfit_share[None], (channels,) + misfit_share.shape)
    gathered = lax.all_to_all(spread, "surface", split_axis=0, concat_axis=0, tiled=True)
    misfit = jnp.moveaxis(gathered, 0, 2).reshape(parts, shots, recvs, freqs)
    misfit_real = misfit[0]
    misfit_imag = misfit[1]
    grad_spectra = jnp.concatenate(
        [
            -(correlate(misfit_real, data_real) + correlate(misfit_imag, data_imag)),
            correlate(misfit_real, data_imag) - correlate(misfit_imag, data_real),
        ],
        axis=-1,
    )
    grad_time = jnp.dot(grad_spectra, dft_table.T, precision=lax.Precision.HIGHEST)
    grad_half = grad_time.astype(jnp.bfloat16)
    returning = jnp.zeros((owners,) + grad_time.shape[1:], jnp.bfloat16).at[own_owner].set(grad_half)
    received = lax.all_to_all(returning, "target", split_axis=0, concat_axis=0, tiled=True)
    flat = received.reshape(owners, -1)
    gradient = jnp.dot(
        picker.astype(jnp.bfloat16), flat, preferred_element_type=jnp.float32
    ).reshape(response.shape)
    response_next = response - step_length * gradient
    return (response_next, response_next.astype(jnp.bfloat16), residual_share[None])


def solution(mesh):
    return jax.shard_map(
        per_device,
        mesh=mesh,
        in_specs=(
            P("target", None, "surface", None),
            P("target", None, None, "surface", None, None),
            P("target", None, None, "surface", None),
            P(),
        ),
        out_specs=(
            P("target", None, "surface", None),
            P("target", None, "surface", None),
            P("target", None, None, "surface", None),
        ),
        check_vma=False,
    )
```

```python
import math

import jax
import jax.numpy as jnp
from jax import lax
from jax.sharding import PartitionSpec as P

step_length = 0.5
chunks = 2


def make_table(samples):
    freqs = samples // 2
    sample_index = lax.broadcasted_iota(jnp.int32, (samples, freqs), 0)
    freq_index = lax.broadcasted_iota(jnp.int32, (samples, freqs), 1)
    phase = (sample_index * freq_index % samples).astype(jnp.float32) * (2.0 * math.pi / samples)
    return jnp.concatenate([jnp.cos(phase), -jnp.sin(phase)], axis=1)


def contract(spec, listed):
    return jnp.einsum("lakf,lkrf->arf", spec, listed, preferred_element_type=jnp.float32)


def correlate(misfit_part, listed):
    return jnp.einsum("arf,lkrf->lakf", misfit_part, listed, preferred_element_type=jnp.float32)


def per_device(response, data_spectra, observed, block_lists):
    owners = lax.axis_size("target")
    channels = lax.axis_size("surface")
    my_index = lax.axis_index("target")
    owned = response.shape[0]
    shots = response.shape[1]
    samples = response.shape[3]
    freqs = samples // 2
    dft_table = make_table(samples)
    table_half = dft_table.astype(jnp.bfloat16)
    own_ids = lax.dynamic_slice_in_dim(block_lists, my_index, 1, 0)[0]
    own_owner = own_ids // owned
    wanted = block_lists // owned == my_index
    present = jnp.any(wanted, axis=1)
    slot_for = jnp.sum(jnp.where(wanted, block_lists % owned, 0), axis=1)
    picker = (
        (slot_for[None, :] == jnp.arange(owned, dtype=jnp.int32)[:, None]) & present[None, :]
    ).astype(jnp.bfloat16)
    present_rows = present[:, None, None, None]
    zero_half = jnp.zeros((), jnp.bfloat16)
    copy_now = response.astype(jnp.bfloat16)
    listed_data = data_spectra[0]
    data_real = listed_data[:, 0]
    data_imag = listed_data[:, 1]
    observed_all = observed[0].astype(jnp.float32)
    width = shots // chunks
    next_parts, copy_parts, residual_parts = [], [], []
    for c in range(chunks):
        lo, hi = c * width, (c + 1) * width
        outgoing = jnp.where(present_rows, copy_now[slot_for, lo:hi], zero_half)
        arrived = lax.all_to_all(outgoing, "target", split_axis=0, concat_axis=0, tiled=True)
        spectra = jnp.dot(arrived[own_owner], table_half, preferred_element_type=jnp.float32).astype(
            jnp.bfloat16
        )
        spec_real = spectra[..., :freqs]
        spec_imag = spectra[..., freqs:]
        partial_value = jnp.stack(
            [
                contract(spec_real, data_real) - contract(spec_imag, data_imag),
                contract(spec_real, data_imag) + contract(spec_imag, data_real),
            ]
        )
        recvs = partial_value.shape[2]
        split_value = partial_value.reshape(2, width, channels, recvs // channels, freqs)
        exchanged = lax.all_to_all(split_value, "surface", split_axis=2, concat_axis=2, tiled=True)
        summed_share = jnp.sum(exchanged, axis=2)
        residual_share = observed_all[:, lo:hi] - summed_share
        misfit_share = residual_share.astype(jnp.bfloat16)
        spread = jnp.broadcast_to(misfit_share[None], (channels,) + misfit_share.shape)
        gathered = lax.all_to_all(spread, "surface", split_axis=0, concat_axis=0, tiled=True)
        misfit = jnp.moveaxis(gathered, 0, 2).reshape(2, width, recvs, freqs)
        misfit_real = misfit[0]
        misfit_imag = misfit[1]
        grad_spectra = jnp.concatenate(
            [
                -(correlate(misfit_real, data_real) + correlate(misfit_imag, data_imag)),
                correlate(misfit_real, data_imag) - correlate(misfit_imag, data_real),
            ],
            axis=-1,
        )
        grad_time = jnp.dot(grad_spectra, dft_table.T, precision=lax.Precision.HIGHEST)
        grad_half = grad_time.astype(jnp.bfloat16)
        returning = jnp.zeros((owners,) + grad_time.shape[1:], jnp.bfloat16).at[own_owner].set(grad_half)
        received = lax.all_to_all(returning, "target", split_axis=0, concat_axis=0, tiled=True)
        flat = received.reshape(owners, -1)
        gradient = jnp.dot(picker, flat, preferred_element_type=jnp.float32).reshape(
            (owned, width) + response.shape[2:]
        )
        response_next = response[:, lo:hi] - step_length * gradient
        next_parts.append(response_next)
        copy_parts.append(response_next.astype(jnp.bfloat16))
        residual_parts.append(residual_share)
    response_next = jnp.concatenate(next_parts, axis=1)
    response_copy = jnp.concatenate(copy_parts, axis=1)
    residual = jnp.concatenate(residual_parts, axis=1)
    return (response_next, response_copy, residual[None])


def solution(mesh):
    return jax.shard_map(
        per_device,
        mesh=mesh,
        in_specs=(
            P("target", None, "surface", None),
            P("target", None, None, "surface", None, None),
            P("target", None, None, "surface", None),
            P(),
        ),
        out_specs=(
            P("target", None, "surface", None),
            P("target", None, "surface", None),
            P("target", None, None, "surface", None),
        ),
        check_vma=False,
    )
```

```python
import math

import jax
import jax.numpy as jnp
from jax import lax
from jax.sharding import PartitionSpec as P

step_length = 0.5


def make_table(samples):
    freqs = samples // 2
    sample_index = lax.broadcasted_iota(jnp.int32, (samples, freqs), 0)
    freq_index = lax.broadcasted_iota(jnp.int32, (samples, freqs), 1)
    phase = (sample_index * freq_index % samples).astype(jnp.float32) * (2.0 * math.pi / samples)
    return jnp.concatenate([jnp.cos(phase), -jnp.sin(phase)], axis=1)


def contract(spec, listed):
    return jnp.einsum("lakf,lkrf->arf", spec, listed, preferred_element_type=jnp.float32)


def correlate(misfit_part, listed):
    return jnp.einsum("arf,lkrf->lakf", misfit_part, listed, preferred_element_type=jnp.float32)


def per_device(response, data_spectra, observed, block_lists):
    owners = lax.axis_size("target")
    channels = lax.axis_size("surface")
    my_index = lax.axis_index("target")
    owned = response.shape[0]
    samples = response.shape[3]
    freqs = samples // 2
    dft_table = make_table(samples)
    table_half = dft_table.astype(jnp.bfloat16).reshape(samples, 2, freqs)
    table_full = dft_table.reshape(samples, 2, freqs)
    own_ids = lax.dynamic_slice_in_dim(block_lists, my_index, 1, 0)[0]
    own_owner = own_ids // owned
    wanted = block_lists // owned == my_index
    present = jnp.any(wanted, axis=1)
    slot_for = jnp.sum(jnp.where(wanted, block_lists % owned, 0), axis=1)
    chosen = (slot_for[None, :] == jnp.arange(owned, dtype=jnp.int32)[:, None]) & present[None, :]
    present_rows = present[:, None, None, None]
    zero_half = jnp.zeros((), jnp.bfloat16)
    copy_now = response.astype(jnp.bfloat16)
    outgoing = jnp.where(present_rows, copy_now[slot_for], zero_half)
    arrived = lax.all_to_all(outgoing, "target", split_axis=0, concat_axis=0, tiled=True)
    data_real = jnp.moveaxis(data_spectra[0, :, 0], -1, 0)
    data_imag = jnp.moveaxis(data_spectra[0, :, 1], -1, 0)
    forward = jnp.stack(
        [jnp.stack([data_real, data_imag], 3), jnp.stack([-data_imag, data_real], 3)], 3
    )
    backward = jnp.stack(
        [jnp.stack([-data_real, -data_imag], 3), jnp.stack([data_imag, -data_real], 3)], 3
    )
    spectra = jnp.einsum(
        "lakn,ncf->flakc", arrived[own_owner], table_half, preferred_element_type=jnp.float32
    ).astype(jnp.bfloat16)
    partial_value = jnp.einsum(
        "flakc,flkcdr->fdar", spectra, forward, preferred_element_type=jnp.float32
    )
    f_dim, parts, shots, recvs = partial_value.shape
    split_value = partial_value.reshape(f_dim, parts, shots, channels, recvs // channels)
    exchanged = lax.all_to_all(split_value, "surface", split_axis=3, concat_axis=3, tiled=True)
    summed_share = jnp.moveaxis(jnp.sum(exchanged, axis=3), 0, -1)
    residual_share = observed[0].astype(jnp.float32) - summed_share
    misfit_share = jnp.moveaxis(residual_share.astype(jnp.bfloat16), -1, 0)
    spread = jnp.broadcast_to(misfit_share[:, :, :, None], misfit_share.shape[:3] + (channels,) + misfit_share.shape[3:])
    gathered = lax.all_to_all(spread, "surface", split_axis=3, concat_axis=3, tiled=True)
    misfit = gathered.reshape(f_dim, parts, shots, recvs)
    grad_spectra = jnp.einsum(
        "fcar,flkecr->flake", misfit, backward, preferred_element_type=jnp.float32
    )
    grad_time = jnp.einsum(
        "flake,nef->lakn", grad_spectra, table_full, precision=lax.Precision.HIGHEST
    )
    grad_half = grad_time.astype(jnp.bfloat16)
    returning = jnp.zeros((owners,) + grad_time.shape[1:], jnp.bfloat16).at[own_owner].set(grad_half)
    received = lax.all_to_all(returning, "target", split_axis=0, concat_axis=0, tiled=True)
    taken = jnp.where(
        chosen[:, :, None, None, None], received[None].astype(jnp.float32), jnp.zeros((), jnp.float32)
    )
    gradient = jnp.sum(taken, axis=1)
    response_next = response - step_length * gradient
    return (response_next, response_next.astype(jnp.bfloat16), residual_share[None])


def solution(mesh):
    return jax.shard_map(
        per_device,
        mesh=mesh,
        in_specs=(
            P("target", None, "surface", None),
            P("target", None, None, "surface", None, None),
            P("target", None, None, "surface", None),
            P(),
        ),
        out_specs=(
            P("target", None, "surface", None),
            P("target", None, "surface", None),
            P("target", None, None, "surface", None),
        ),
        check_vma=False,
    )
```

```python
import math

import jax
import jax.numpy as jnp
from jax import lax
from jax.sharding import PartitionSpec as P

step_length = 0.5


def make_table(samples):
    freqs = samples // 2
    sample_index = lax.broadcasted_iota(jnp.int32, (samples, freqs), 0)
    freq_index = lax.broadcasted_iota(jnp.int32, (samples, freqs), 1)
    phase = (sample_index * freq_index % samples).astype(jnp.float32) * (2.0 * math.pi / samples)
    return jnp.concatenate([jnp.cos(phase), -jnp.sin(phase)], axis=1)


def contract(spec, listed):
    return jnp.einsum("lakf,lkrf->arf", spec, listed, preferred_element_type=jnp.float32)


def correlate(misfit_part, listed):
    return jnp.einsum("arf,lkrf->lakf", misfit_part, listed, preferred_element_type=jnp.float32)


def per_device(response, data_spectra, observed, block_lists):
    owners = lax.axis_size("target")
    channels = lax.axis_size("surface")
    my_index = lax.axis_index("target")
    owned = response.shape[0]
    samples = response.shape[3]
    freqs = samples // 2
    dft_table = make_table(samples)
    table_half = dft_table.astype(jnp.bfloat16).reshape(samples, 2, freqs)
    own_ids = lax.dynamic_slice_in_dim(block_lists, my_index, 1, 0)[0]
    own_owner = own_ids // owned
    wanted = block_lists // owned == my_index
    present = jnp.any(wanted, axis=1)
    slot_for = jnp.sum(jnp.where(wanted, block_lists % owned, 0), axis=1)
    chosen = (slot_for[None, :] == jnp.arange(owned, dtype=jnp.int32)[:, None]) & present[None, :]
    present_rows = present[:, None, None, None]
    zero_half = jnp.zeros((), jnp.bfloat16)
    copy_now = response.astype(jnp.bfloat16)
    outgoing = jnp.where(present_rows, copy_now[slot_for], zero_half)
    arrived = lax.all_to_all(outgoing, "target", split_axis=0, concat_axis=0, tiled=True)
    data_real = jnp.moveaxis(data_spectra[0, :, 0], -1, 0)
    data_imag = jnp.moveaxis(data_spectra[0, :, 1], -1, 0)
    forward = jnp.stack(
        [jnp.stack([data_real, data_imag], 3), jnp.stack([-data_imag, data_real], 3)], 3
    )
    backward = jnp.stack(
        [jnp.stack([-data_real, -data_imag], 3), jnp.stack([data_imag, -data_real], 3)], 3
    )
    spectra = jnp.einsum(
        "lakn,ncf->flakc", arrived[own_owner], table_half, preferred_element_type=jnp.float32
    ).astype(jnp.bfloat16)
    partial_value = jnp.einsum(
        "flakc,flkcdr->fdar", spectra, forward, preferred_element_type=jnp.float32
    )
    f_dim, parts, shots, recvs = partial_value.shape
    split_value = partial_value.reshape(f_dim, parts, shots, channels, recvs // channels)
    exchanged = lax.all_to_all(split_value, "surface", split_axis=3, concat_axis=3, tiled=True)
    summed_share = jnp.moveaxis(jnp.sum(exchanged, axis=3), 0, -1)
    residual_share = observed[0].astype(jnp.float32) - summed_share
    misfit_share = jnp.moveaxis(residual_share.astype(jnp.bfloat16), -1, 0)
    spread = jnp.broadcast_to(misfit_share[:, :, :, None], misfit_share.shape[:3] + (channels,) + misfit_share.shape[3:])
    gathered = lax.all_to_all(spread, "surface", split_axis=3, concat_axis=3, tiled=True)
    misfit = gathered.reshape(f_dim, parts, shots, recvs)
    grad_spectra = jnp.einsum(
        "fcar,flkecr->lakef", misfit, backward, preferred_element_type=jnp.float32
    )
    grad_flat = grad_spectra.reshape(grad_spectra.shape[:3] + (samples,))
    grad_time = jnp.dot(grad_flat, dft_table.T, precision=lax.Precision.HIGHEST)
    grad_half = grad_time.astype(jnp.bfloat16)
    returning = jnp.zeros((owners,) + grad_time.shape[1:], jnp.bfloat16).at[own_owner].set(grad_half)
    received = lax.all_to_all(returning, "target", split_axis=0, concat_axis=0, tiled=True)
    taken = jnp.where(
        chosen[:, :, None, None, None], received[None].astype(jnp.float32), jnp.zeros((), jnp.float32)
    )
    gradient = jnp.sum(taken, axis=1)
    response_next = response - step_length * gradient
    return (response_next, response_next.astype(jnp.bfloat16), residual_share[None])


def solution(mesh):
    return jax.shard_map(
        per_device,
        mesh=mesh,
        in_specs=(
            P("target", None, "surface", None),
            P("target", None, None, "surface", None, None),
            P("target", None, None, "surface", None),
            P(),
        ),
        out_specs=(
            P("target", None, "surface", None),
            P("target", None, "surface", None),
            P("target", None, None, "surface", None),
        ),
        check_vma=False,
    )
```

```python
import math

import jax
import jax.numpy as jnp
from jax import lax
from jax.sharding import PartitionSpec as P

step_length = 0.5
chunks = 2


def make_table(samples):
    freqs = samples // 2
    sample_index = lax.broadcasted_iota(jnp.int32, (samples, freqs), 0)
    freq_index = lax.broadcasted_iota(jnp.int32, (samples, freqs), 1)
    phase = (sample_index * freq_index % samples).astype(jnp.float32) * (2.0 * math.pi / samples)
    return jnp.concatenate([jnp.cos(phase), -jnp.sin(phase)], axis=1)


def contract(spec, listed):
    return jnp.einsum("lakf,lkrf->arf", spec, listed, preferred_element_type=jnp.float32)


def correlate(misfit_part, listed):
    return jnp.einsum("arf,lkrf->lakf", misfit_part, listed, preferred_element_type=jnp.float32)


def per_device(response, data_spectra, observed, block_lists):
    owners = lax.axis_size("target")
    channels = lax.axis_size("surface")
    my_index = lax.axis_index("target")
    owned = response.shape[0]
    samples = response.shape[3]
    freqs = samples // 2
    dft_table = make_table(samples)
    table_half = dft_table.astype(jnp.bfloat16).reshape(samples, 2, freqs)
    own_ids = lax.dynamic_slice_in_dim(block_lists, my_index, 1, 0)[0]
    own_owner = own_ids // owned
    wanted = block_lists // owned == my_index
    present = jnp.any(wanted, axis=1)
    slot_for = jnp.sum(jnp.where(wanted, block_lists % owned, 0), axis=1)
    chosen = (slot_for[None, :] == jnp.arange(owned, dtype=jnp.int32)[:, None]) & present[None, :]
    present_rows = present[:, None, None, None]
    zero_half = jnp.zeros((), jnp.bfloat16)
    copy_now = response.astype(jnp.bfloat16)
    outgoing = jnp.where(present_rows, copy_now[slot_for], zero_half)
    arrived = lax.all_to_all(outgoing, "target", split_axis=0, concat_axis=0, tiled=True) if chunks == 1 else None
    data_real = jnp.moveaxis(data_spectra[0, :, 0], -1, 0)
    data_imag = jnp.moveaxis(data_spectra[0, :, 1], -1, 0)
    forward = jnp.stack(
        [jnp.stack([data_real, data_imag], 3), jnp.stack([-data_imag, data_real], 3)], 3
    )
    backward = jnp.stack(
        [jnp.stack([-data_real, -data_imag], 3), jnp.stack([data_imag, -data_real], 3)], 3
    )
    positions = response.shape[2]
    width = positions // chunks
    partial_value = None
    for c in range(chunks):
        lo, hi = c * width, (c + 1) * width
        piece = outgoing if chunks == 1 else outgoing[:, :, lo:hi]
        arrived_c = arrived if chunks == 1 else lax.all_to_all(
            piece, "target", split_axis=0, concat_axis=0, tiled=True
        )
        spectra = jnp.einsum(
            "lakn,ncf->flakc", arrived_c[own_owner], table_half, preferred_element_type=jnp.float32
        ).astype(jnp.bfloat16)
        partial_c = jnp.einsum(
            "flakc,flkcdr->fdar", spectra, forward[:, :, lo:hi], preferred_element_type=jnp.float32
        )
        partial_value = partial_c if partial_value is None else partial_value + partial_c
    f_dim, parts, shots, recvs = partial_value.shape
    split_value = partial_value.reshape(f_dim, parts, shots, channels, recvs // channels)
    exchanged = lax.all_to_all(split_value, "surface", split_axis=3, concat_axis=3, tiled=True)
    summed_share = jnp.moveaxis(jnp.sum(exchanged, axis=3), 0, -1)
    residual_share = observed[0].astype(jnp.float32) - summed_share
    misfit_share = jnp.moveaxis(residual_share.astype(jnp.bfloat16), -1, 0)
    spread = jnp.broadcast_to(misfit_share[:, :, :, None], misfit_share.shape[:3] + (channels,) + misfit_share.shape[3:])
    gathered = lax.all_to_all(spread, "surface", split_axis=3, concat_axis=3, tiled=True)
    misfit = gathered.reshape(f_dim, parts, shots, recvs)
    next_parts = []
    for c in range(chunks):
        lo, hi = c * width, (c + 1) * width
        grad_spectra = jnp.einsum(
            "fcar,flkecr->lakef", misfit, backward[:, :, lo:hi], preferred_element_type=jnp.float32
        )
        grad_flat = grad_spectra.reshape(grad_spectra.shape[:3] + (samples,))
        grad_time = jnp.dot(grad_flat, dft_table.T, precision=lax.Precision.HIGHEST)
        grad_half = grad_time.astype(jnp.bfloat16)
        returning = jnp.zeros((owners,) + grad_time.shape[1:], jnp.bfloat16).at[own_owner].set(grad_half)
        received = lax.all_to_all(returning, "target", split_axis=0, concat_axis=0, tiled=True)
        taken = jnp.where(
            chosen[:, :, None, None, None], received[None].astype(jnp.float32), jnp.zeros((), jnp.float32)
        )
        gradient = jnp.sum(taken, axis=1)
        next_parts.append(response[:, :, lo:hi] - step_length * gradient)
    response_next = next_parts[0] if chunks == 1 else jnp.concatenate(next_parts, axis=2)
    return (response_next, response_next.astype(jnp.bfloat16), residual_share[None])


def solution(mesh):
    return jax.shard_map(
        per_device,
        mesh=mesh,
        in_specs=(
            P("target", None, "surface", None),
            P("target", None, None, "surface", None, None),
            P("target", None, None, "surface", None),
            P(),
        ),
        out_specs=(
            P("target", None, "surface", None),
            P("target", None, "surface", None),
            P("target", None, None, "surface", None),
        ),
        check_vma=False,
    )
```

```python
import math

import jax
import jax.numpy as jnp
from jax import lax
from jax.sharding import PartitionSpec as P

step_length = 0.5


def make_table(samples):
    freqs = samples // 2
    sample_index = lax.broadcasted_iota(jnp.int32, (samples, freqs), 0)
    freq_index = lax.broadcasted_iota(jnp.int32, (samples, freqs), 1)
    phase = (sample_index * freq_index % samples).astype(jnp.float32) * (2.0 * math.pi / samples)
    return jnp.concatenate([jnp.cos(phase), -jnp.sin(phase)], axis=1)


def contract(spec, listed):
    return jnp.einsum("lakf,lkrf->arf", spec, listed, preferred_element_type=jnp.float32)


def correlate(misfit_part, listed):
    return jnp.einsum("arf,lkrf->lakf", misfit_part, listed, preferred_element_type=jnp.float32)


def per_device(response, data_spectra, observed, block_lists):
    owners = lax.axis_size("target")
    channels = lax.axis_size("surface")
    my_index = lax.axis_index("target")
    owned = response.shape[0]
    samples = response.shape[3]
    freqs = samples // 2
    dft_table = make_table(samples)
    table_half = dft_table.astype(jnp.bfloat16).reshape(samples, 2, freqs)
    own_ids = lax.dynamic_slice_in_dim(block_lists, my_index, 1, 0)[0]
    own_owner = own_ids // owned
    wanted = block_lists // owned == my_index
    present = jnp.any(wanted, axis=1)
    slot_for = jnp.sum(jnp.where(wanted, block_lists % owned, 0), axis=1)
    chosen = (slot_for[None, :] == jnp.arange(owned, dtype=jnp.int32)[:, None]) & present[None, :]
    present_rows = present[:, None, None, None]
    zero_half = jnp.zeros((), jnp.bfloat16)
    copy_now = response.astype(jnp.bfloat16)
    outgoing = jnp.where(present_rows, copy_now[slot_for], zero_half)
    arrived = lax.all_to_all(outgoing, "target", split_axis=0, concat_axis=0, tiled=True)
    data_real = jnp.moveaxis(data_spectra[0, :, 0], -1, 0)
    data_imag = jnp.moveaxis(data_spectra[0, :, 1], -1, 0)
    forward = jnp.stack(
        [jnp.stack([data_real, data_imag], 3), jnp.stack([-data_imag, data_real], 3)], 3
    )
    backward = jnp.stack(
        [jnp.stack([-data_real, -data_imag], 3), jnp.stack([data_imag, -data_real], 3)], 3
    )
    spectra = jnp.einsum(
        "lakn,ncf->flakc", arrived[own_owner], table_half, preferred_element_type=jnp.float32
    ).astype(jnp.bfloat16)
    partial_value = jnp.einsum(
        "flakc,flkcdr->fdar", spectra, forward, preferred_element_type=jnp.float32
    )
    f_dim, parts, shots, recvs = partial_value.shape
    split_value = partial_value.reshape(f_dim, parts, shots, channels, recvs // channels)
    exchanged = lax.all_to_all(
        split_value.astype(jnp.bfloat16), "surface", split_axis=3, concat_axis=3, tiled=True
    )
    summed_share = jnp.moveaxis(jnp.sum(exchanged.astype(jnp.float32), axis=3), 0, -1)
    residual_share = observed[0].astype(jnp.float32) - summed_share
    misfit_share = jnp.moveaxis(residual_share.astype(jnp.bfloat16), -1, 0)
    spread = jnp.broadcast_to(misfit_share[:, :, :, None], misfit_share.shape[:3] + (channels,) + misfit_share.shape[3:])
    gathered = lax.all_to_all(spread, "surface", split_axis=3, concat_axis=3, tiled=True)
    misfit = gathered.reshape(f_dim, parts, shots, recvs)
    grad_spectra = jnp.einsum(
        "fcar,flkecr->lakef", misfit, backward, preferred_element_type=jnp.float32
    )
    grad_flat = grad_spectra.reshape(grad_spectra.shape[:3] + (samples,))
    grad_time = jnp.dot(grad_flat, dft_table.T, precision=lax.Precision.HIGHEST)
    grad_half = grad_time.astype(jnp.bfloat16)
    returning = jnp.zeros((owners,) + grad_time.shape[1:], jnp.bfloat16).at[own_owner].set(grad_half)
    received = lax.all_to_all(returning, "target", split_axis=0, concat_axis=0, tiled=True)
    taken = jnp.where(
        chosen[:, :, None, None, None], received[None].astype(jnp.float32), jnp.zeros((), jnp.float32)
    )
    gradient = jnp.sum(taken, axis=1)
    response_next = response - step_length * gradient
    return (response_next, response_next.astype(jnp.bfloat16), residual_share[None])


def solution(mesh):
    return jax.shard_map(
        per_device,
        mesh=mesh,
        in_specs=(
            P("target", None, "surface", None),
            P("target", None, None, "surface", None, None),
            P("target", None, None, "surface", None),
            P(),
        ),
        out_specs=(
            P("target", None, "surface", None),
            P("target", None, "surface", None),
            P("target", None, None, "surface", None),
        ),
        check_vma=False,
    )
```

```python
import math

import jax
import jax.numpy as jnp
from jax import lax
from jax.sharding import PartitionSpec as P

step_length = 0.5


def make_table(samples):
    freqs = samples // 2
    sample_index = lax.broadcasted_iota(jnp.int32, (samples, freqs), 0)
    freq_index = lax.broadcasted_iota(jnp.int32, (samples, freqs), 1)
    phase = (sample_index * freq_index % samples).astype(jnp.float32) * (2.0 * math.pi / samples)
    return jnp.concatenate([jnp.cos(phase), -jnp.sin(phase)], axis=1)


def contract(spec, listed):
    return jnp.einsum("lakf,lkrf->arf", spec, listed, preferred_element_type=jnp.float32)


def correlate(misfit_part, listed):
    return jnp.einsum("arf,lkrf->lakf", misfit_part, listed, preferred_element_type=jnp.float32)


def per_device(response, data_spectra, observed, block_lists):
    owners = lax.axis_size("target")
    channels = lax.axis_size("surface")
    my_index = lax.axis_index("target")
    owned = response.shape[0]
    samples = response.shape[3]
    freqs = samples // 2
    dft_table = make_table(samples)
    table_half = dft_table.astype(jnp.bfloat16).reshape(samples, 2, freqs)
    own_ids = lax.dynamic_slice_in_dim(block_lists, my_index, 1, 0)[0]
    own_owner = own_ids // owned
    wanted = block_lists // owned == my_index
    present = jnp.any(wanted, axis=1)
    slot_for = jnp.sum(jnp.where(wanted, block_lists % owned, 0), axis=1)
    chosen = (slot_for[None, :] == jnp.arange(owned, dtype=jnp.int32)[:, None]) & present[None, :]
    copy_now = response.astype(jnp.bfloat16)
    outgoing = copy_now[slot_for]
    arrived = lax.all_to_all(outgoing, "target", split_axis=0, concat_axis=0, tiled=True)
    data_real = jnp.moveaxis(data_spectra[0, :, 0], -1, 0)
    data_imag = jnp.moveaxis(data_spectra[0, :, 1], -1, 0)
    forward = jnp.stack(
        [jnp.stack([data_real, data_imag], 3), jnp.stack([-data_imag, data_real], 3)], 3
    )
    backward = jnp.stack(
        [jnp.stack([-data_real, -data_imag], 3), jnp.stack([data_imag, -data_real], 3)], 3
    )
    spectra = jnp.einsum(
        "lakn,ncf->flakc", arrived[own_owner], table_half, preferred_element_type=jnp.float32
    ).astype(jnp.bfloat16)
    partial_value = jnp.einsum(
        "flakc,flkcdr->fdar", spectra, forward, preferred_element_type=jnp.float32
    )
    f_dim, parts, shots, recvs = partial_value.shape
    split_value = partial_value.reshape(f_dim, parts, shots, channels, recvs // channels)
    exchanged = lax.all_to_all(split_value, "surface", split_axis=3, concat_axis=3, tiled=True)
    summed_share = jnp.moveaxis(jnp.sum(exchanged, axis=3), 0, -1)
    residual_share = observed[0].astype(jnp.float32) - summed_share
    misfit_share = jnp.moveaxis(residual_share.astype(jnp.bfloat16), -1, 0)
    spread = jnp.broadcast_to(misfit_share[:, :, :, None], misfit_share.shape[:3] + (channels,) + misfit_share.shape[3:])
    gathered = lax.all_to_all(spread, "surface", split_axis=3, concat_axis=3, tiled=True)
    misfit = gathered.reshape(f_dim, parts, shots, recvs)
    grad_spectra = jnp.einsum(
        "fcar,flkecr->lakef", misfit, backward, preferred_element_type=jnp.float32
    )
    grad_flat = grad_spectra.reshape(grad_spectra.shape[:3] + (samples,))
    grad_time = jnp.dot(grad_flat, dft_table.T, precision=lax.Precision.HIGHEST)
    grad_half = grad_time.astype(jnp.bfloat16)
    match = own_owner[None, :] == jnp.arange(owners, dtype=jnp.int32)[:, None]
    entry_for = jnp.argmax(match, axis=1)
    returning = grad_half[entry_for]
    received = lax.all_to_all(returning, "target", split_axis=0, concat_axis=0, tiled=True)
    taken = jnp.where(
        chosen[:, :, None, None, None], received[None].astype(jnp.float32), jnp.zeros((), jnp.float32)
    )
    gradient = jnp.sum(taken, axis=1)
    response_next = response - step_length * gradient
    return (response_next, response_next.astype(jnp.bfloat16), residual_share[None])


def solution(mesh):
    return jax.shard_map(
        per_device,
        mesh=mesh,
        in_specs=(
            P("target", None, "surface", None),
            P("target", None, None, "surface", None, None),
            P("target", None, None, "surface", None),
            P(),
        ),
        out_specs=(
            P("target", None, "surface", None),
            P("target", None, "surface", None),
            P("target", None, None, "surface", None),
        ),
        check_vma=False,
    )
```

```python
import math

import jax
import jax.numpy as jnp
from jax import lax
from jax.sharding import PartitionSpec as P

step_length = 0.5


def make_table(samples):
    freqs = samples // 2
    sample_index = lax.broadcasted_iota(jnp.int32, (samples, freqs), 0)
    freq_index = lax.broadcasted_iota(jnp.int32, (samples, freqs), 1)
    phase = (sample_index * freq_index % samples).astype(jnp.float32) * (2.0 * math.pi / samples)
    return jnp.concatenate([jnp.cos(phase), -jnp.sin(phase)], axis=1)


def contract(spec, listed):
    return jnp.einsum("lakf,lkrf->arf", spec, listed, preferred_element_type=jnp.float32)


def correlate(misfit_part, listed):
    return jnp.einsum("arf,lkrf->lakf", misfit_part, listed, preferred_element_type=jnp.float32)


def per_device(response, data_spectra, observed, block_lists):
    owners = lax.axis_size("target")
    channels = lax.axis_size("surface")
    my_index = lax.axis_index("target")
    owned = response.shape[0]
    samples = response.shape[3]
    freqs = samples // 2
    dft_table = make_table(samples)
    table_half = dft_table.astype(jnp.bfloat16).reshape(samples, 2, freqs)
    own_ids = lax.dynamic_slice_in_dim(block_lists, my_index, 1, 0)[0]
    own_owner = own_ids // owned
    wanted = block_lists // owned == my_index
    present = jnp.any(wanted, axis=1)
    slot_for = jnp.sum(jnp.where(wanted, block_lists % owned, 0), axis=1)
    chosen = (slot_for[None, :] == jnp.arange(owned, dtype=jnp.int32)[:, None]) & present[None, :]
    copy_now = response.astype(jnp.bfloat16)
    outgoing = copy_now[slot_for]
    arrived = lax.all_to_all(outgoing, "target", split_axis=0, concat_axis=0, tiled=True)
    data_real = jnp.moveaxis(data_spectra[0, :, 0], -1, 0)
    data_imag = jnp.moveaxis(data_spectra[0, :, 1], -1, 0)
    forward = jnp.stack(
        [jnp.stack([data_real, data_imag], 3), jnp.stack([-data_imag, data_real], 3)], 3
    )
    backward = jnp.stack(
        [jnp.stack([-data_real, -data_imag], 3), jnp.stack([data_imag, -data_real], 3)], 3
    )
    spectra = jnp.einsum(
        "lakn,ncf->flakc", arrived[own_owner], table_half, preferred_element_type=jnp.float32
    ).astype(jnp.bfloat16)
    partial_value = jnp.einsum(
        "flakc,flkcdr->fdar", spectra, forward, preferred_element_type=jnp.float32
    )
    f_dim, parts, shots, recvs = partial_value.shape
    split_value = partial_value.reshape(f_dim, parts, shots, channels, recvs // channels)
    exchanged = lax.all_to_all(split_value, "surface", split_axis=3, concat_axis=3, tiled=True)
    summed_share = jnp.moveaxis(jnp.sum(exchanged, axis=3), 0, -1)
    residual_share = observed[0].astype(jnp.float32) - summed_share
    misfit_share = jnp.moveaxis(residual_share.astype(jnp.bfloat16), -1, 0)
    spread = jnp.broadcast_to(misfit_share[:, :, :, None], misfit_share.shape[:3] + (channels,) + misfit_share.shape[3:])
    gathered = lax.all_to_all(spread, "surface", split_axis=3, concat_axis=3, tiled=True)
    misfit = gathered.reshape(f_dim, parts, shots, recvs)
    grad_spectra = jnp.einsum(
        "fcar,flkecr->lakef", misfit, backward, preferred_element_type=jnp.float32
    )
    grad_flat = grad_spectra.reshape(grad_spectra.shape[:3] + (samples,))
    grad_time = jnp.dot(grad_flat, dft_table.T, precision=lax.Precision.HIGH)
    grad_half = grad_time.astype(jnp.bfloat16)
    match = own_owner[None, :] == jnp.arange(owners, dtype=jnp.int32)[:, None]
    entry_for = jnp.argmax(match, axis=1)
    returning = grad_half[entry_for]
    received = lax.all_to_all(returning, "target", split_axis=0, concat_axis=0, tiled=True)
    taken = jnp.where(
        chosen[:, :, None, None, None], received[None].astype(jnp.float32), jnp.zeros((), jnp.float32)
    )
    gradient = jnp.sum(taken, axis=1)
    response_next = response - step_length * gradient
    return (response_next, response_next.astype(jnp.bfloat16), residual_share[None])


def solution(mesh):
    return jax.shard_map(
        per_device,
        mesh=mesh,
        in_specs=(
            P("target", None, "surface", None),
            P("target", None, None, "surface", None, None),
            P("target", None, None, "surface", None),
            P(),
        ),
        out_specs=(
            P("target", None, "surface", None),
            P("target", None, "surface", None),
            P("target", None, None, "surface", None),
        ),
        check_vma=False,
    )
```

```python
import math

import jax
import jax.numpy as jnp
from jax import lax
from jax.sharding import PartitionSpec as P

step_length = 0.5
chunks = 2


def make_table(samples):
    freqs = samples // 2
    sample_index = lax.broadcasted_iota(jnp.int32, (samples, freqs), 0)
    freq_index = lax.broadcasted_iota(jnp.int32, (samples, freqs), 1)
    phase = (sample_index * freq_index % samples).astype(jnp.float32) * (2.0 * math.pi / samples)
    return jnp.concatenate([jnp.cos(phase), -jnp.sin(phase)], axis=1)


def contract(spec, listed):
    return jnp.einsum("lakf,lkrf->arf", spec, listed, preferred_element_type=jnp.float32)


def correlate(misfit_part, listed):
    return jnp.einsum("arf,lkrf->lakf", misfit_part, listed, preferred_element_type=jnp.float32)


def per_device(response, data_spectra, observed, block_lists):
    owners = lax.axis_size("target")
    channels = lax.axis_size("surface")
    my_index = lax.axis_index("target")
    owned = response.shape[0]
    samples = response.shape[3]
    freqs = samples // 2
    dft_table = make_table(samples)
    table_half = dft_table.astype(jnp.bfloat16).reshape(samples, 2, freqs)
    own_ids = lax.dynamic_slice_in_dim(block_lists, my_index, 1, 0)[0]
    own_owner = own_ids // owned
    wanted = block_lists // owned == my_index
    present = jnp.any(wanted, axis=1)
    slot_for = jnp.sum(jnp.where(wanted, block_lists % owned, 0), axis=1)
    chosen = (slot_for[None, :] == jnp.arange(owned, dtype=jnp.int32)[:, None]) & present[None, :]
    copy_now = response.astype(jnp.bfloat16)
    outgoing = copy_now[slot_for]
    arrived = lax.all_to_all(outgoing, "target", split_axis=0, concat_axis=0, tiled=True)
    data_real = jnp.moveaxis(data_spectra[0, :, 0], -1, 0)
    data_imag = jnp.moveaxis(data_spectra[0, :, 1], -1, 0)
    forward = jnp.stack(
        [jnp.stack([data_real, data_imag], 3), jnp.stack([-data_imag, data_real], 3)], 3
    )
    backward = jnp.stack(
        [jnp.stack([-data_real, -data_imag], 3), jnp.stack([data_imag, -data_real], 3)], 3
    )
    spectra = jnp.einsum(
        "lakn,ncf->flakc", arrived[own_owner], table_half, preferred_element_type=jnp.float32
    ).astype(jnp.bfloat16)
    partial_value = jnp.einsum(
        "flakc,flkcdr->fdar", spectra, forward, preferred_element_type=jnp.float32
    )
    f_dim, parts, shots, recvs = partial_value.shape
    split_value = partial_value.reshape(f_dim, parts, shots, channels, recvs // channels)
    exchanged = lax.all_to_all(split_value, "surface", split_axis=3, concat_axis=3, tiled=True)
    summed_share = jnp.moveaxis(jnp.sum(exchanged, axis=3), 0, -1)
    residual_share = observed[0].astype(jnp.float32) - summed_share
    misfit_share = jnp.moveaxis(residual_share.astype(jnp.bfloat16), -1, 0)
    spread = jnp.broadcast_to(misfit_share[:, :, :, None], misfit_share.shape[:3] + (channels,) + misfit_share.shape[3:])
    gathered = lax.all_to_all(spread, "surface", split_axis=3, concat_axis=3, tiled=True)
    misfit = gathered.reshape(f_dim, parts, shots, recvs)
    match = own_owner[None, :] == jnp.arange(owners, dtype=jnp.int32)[:, None]
    entry_for = jnp.argmax(match, axis=1)
    positions = response.shape[2]
    width = positions // chunks
    next_parts = []
    for c in range(chunks):
        lo, hi = c * width, (c + 1) * width
        grad_spectra = jnp.einsum(
            "fcar,flkecr->lakef", misfit, backward[:, :, lo:hi], preferred_element_type=jnp.float32
        )
        grad_flat = grad_spectra.reshape(grad_spectra.shape[:3] + (samples,))
        grad_time = jnp.dot(grad_flat, dft_table.T, precision=lax.Precision.HIGH)
        returning = grad_time.astype(jnp.bfloat16)[entry_for]
        received = lax.all_to_all(returning, "target", split_axis=0, concat_axis=0, tiled=True)
        taken = jnp.where(
            chosen[:, :, None, None, None], received[None].astype(jnp.float32), jnp.zeros((), jnp.float32)
        )
        gradient = jnp.sum(taken, axis=1)
        next_parts.append(response[:, :, lo:hi] - step_length * gradient)
    response_next = next_parts[0] if chunks == 1 else jnp.concatenate(next_parts, axis=2)
    return (response_next, response_next.astype(jnp.bfloat16), residual_share[None])


def solution(mesh):
    return jax.shard_map(
        per_device,
        mesh=mesh,
        in_specs=(
            P("target", None, "surface", None),
            P("target", None, None, "surface", None, None),
            P("target", None, None, "surface", None),
            P(),
        ),
        out_specs=(
            P("target", None, "surface", None),
            P("target", None, "surface", None),
            P("target", None, None, "surface", None),
        ),
        check_vma=False,
    )
```

```python
import math

import jax
import jax.numpy as jnp
from jax import lax
from jax.sharding import PartitionSpec as P

step_length = 0.5
chunks = 4


def make_table(samples):
    freqs = samples // 2
    sample_index = lax.broadcasted_iota(jnp.int32, (samples, freqs), 0)
    freq_index = lax.broadcasted_iota(jnp.int32, (samples, freqs), 1)
    phase = (sample_index * freq_index % samples).astype(jnp.float32) * (2.0 * math.pi / samples)
    return jnp.concatenate([jnp.cos(phase), -jnp.sin(phase)], axis=1)


def contract(spec, listed):
    return jnp.einsum("lakf,lkrf->arf", spec, listed, preferred_element_type=jnp.float32)


def correlate(misfit_part, listed):
    return jnp.einsum("arf,lkrf->lakf", misfit_part, listed, preferred_element_type=jnp.float32)


def per_device(response, data_spectra, observed, block_lists):
    owners = lax.axis_size("target")
    channels = lax.axis_size("surface")
    my_index = lax.axis_index("target")
    owned = response.shape[0]
    samples = response.shape[3]
    freqs = samples // 2
    dft_table = make_table(samples)
    table_half = dft_table.astype(jnp.bfloat16).reshape(samples, 2, freqs)
    own_ids = lax.dynamic_slice_in_dim(block_lists, my_index, 1, 0)[0]
    own_owner = own_ids // owned
    wanted = block_lists // owned == my_index
    present = jnp.any(wanted, axis=1)
    slot_for = jnp.sum(jnp.where(wanted, block_lists % owned, 0), axis=1)
    chosen = (slot_for[None, :] == jnp.arange(owned, dtype=jnp.int32)[:, None]) & present[None, :]
    copy_now = response.astype(jnp.bfloat16)
    outgoing = copy_now[slot_for]
    arrived = lax.all_to_all(outgoing, "target", split_axis=0, concat_axis=0, tiled=True)
    data_real = jnp.moveaxis(data_spectra[0, :, 0], -1, 0)
    data_imag = jnp.moveaxis(data_spectra[0, :, 1], -1, 0)
    forward = jnp.stack(
        [jnp.stack([data_real, data_imag], 3), jnp.stack([-data_imag, data_real], 3)], 3
    )
    backward = jnp.stack(
        [jnp.stack([-data_real, -data_imag], 3), jnp.stack([data_imag, -data_real], 3)], 3
    )
    spectra = jnp.einsum(
        "lakn,ncf->flakc", arrived[own_owner], table_half, preferred_element_type=jnp.float32
    ).astype(jnp.bfloat16)
    partial_value = jnp.einsum(
        "flakc,flkcdr->fdar", spectra, forward, preferred_element_type=jnp.float32
    )
    f_dim, parts, shots, recvs = partial_value.shape
    split_value = partial_value.reshape(f_dim, parts, shots, channels, recvs // channels)
    exchanged = lax.all_to_all(split_value, "surface", split_axis=3, concat_axis=3, tiled=True)
    summed_share = jnp.moveaxis(jnp.sum(exchanged, axis=3), 0, -1)
    residual_share = observed[0].astype(jnp.float32) - summed_share
    misfit_share = jnp.moveaxis(residual_share.astype(jnp.bfloat16), -1, 0)
    spread = jnp.broadcast_to(misfit_share[:, :, :, None], misfit_share.shape[:3] + (channels,) + misfit_share.shape[3:])
    gathered = lax.all_to_all(spread, "surface", split_axis=3, concat_axis=3, tiled=True)
    misfit = gathered.reshape(f_dim, parts, shots, recvs)
    match = own_owner[None, :] == jnp.arange(owners, dtype=jnp.int32)[:, None]
    entry_for = jnp.argmax(match, axis=1)
    positions = response.shape[2]
    width = positions // chunks
    next_parts = []
    for c in range(chunks):
        lo, hi = c * width, (c + 1) * width
        grad_spectra = jnp.einsum(
            "fcar,flkecr->lakef", misfit, backward[:, :, lo:hi], preferred_element_type=jnp.float32
        )
        grad_flat = grad_spectra.reshape(grad_spectra.shape[:3] + (samples,))
        grad_time = jnp.dot(grad_flat, dft_table.T, precision=lax.Precision.HIGH)
        returning = grad_time.astype(jnp.bfloat16)[entry_for]
        received = lax.all_to_all(returning, "target", split_axis=0, concat_axis=0, tiled=True)
        taken = jnp.where(
            chosen[:, :, None, None, None], received[None].astype(jnp.float32), jnp.zeros((), jnp.float32)
        )
        gradient = jnp.sum(taken, axis=1)
        next_parts.append(response[:, :, lo:hi] - step_length * gradient)
    response_next = next_parts[0] if chunks == 1 else jnp.concatenate(next_parts, axis=2)
    return (response_next, response_next.astype(jnp.bfloat16), residual_share[None])


def solution(mesh):
    return jax.shard_map(
        per_device,
        mesh=mesh,
        in_specs=(
            P("target", None, "surface", None),
            P("target", None, None, "surface", None, None),
            P("target", None, None, "surface", None),
            P(),
        ),
        out_specs=(
            P("target", None, "surface", None),
            P("target", None, "surface", None),
            P("target", None, None, "surface", None),
        ),
        check_vma=False,
    )
```

```python
import math

import jax
import jax.numpy as jnp
from jax import lax
from jax.sharding import PartitionSpec as P

step_length = 0.5
chunks = 2


def make_table(samples):
    freqs = samples // 2
    sample_index = lax.broadcasted_iota(jnp.int32, (samples, freqs), 0)
    freq_index = lax.broadcasted_iota(jnp.int32, (samples, freqs), 1)
    phase = (sample_index * freq_index % samples).astype(jnp.float32) * (2.0 * math.pi / samples)
    return jnp.concatenate([jnp.cos(phase), -jnp.sin(phase)], axis=1)


def contract(spec, listed):
    return jnp.einsum("lakf,lkrf->arf", spec, listed, preferred_element_type=jnp.float32)


def correlate(misfit_part, listed):
    return jnp.einsum("arf,lkrf->lakf", misfit_part, listed, preferred_element_type=jnp.float32)


def per_device(response, data_spectra, observed, block_lists):
    owners = lax.axis_size("target")
    channels = lax.axis_size("surface")
    my_index = lax.axis_index("target")
    owned = response.shape[0]
    samples = response.shape[3]
    freqs = samples // 2
    dft_table = make_table(samples)
    own_ids = lax.dynamic_slice_in_dim(block_lists, my_index, 1, 0)[0]
    own_owner = own_ids // owned
    wanted = block_lists // owned == my_index
    present = jnp.any(wanted, axis=1)
    slot_for = jnp.sum(jnp.where(wanted, block_lists % owned, 0), axis=1)
    chosen = (slot_for[None, :] == jnp.arange(owned, dtype=jnp.int32)[:, None]) & present[None, :]
    copy_now = response.astype(jnp.bfloat16)
    own_spectra = jnp.dot(
        copy_now, dft_table.astype(jnp.bfloat16), preferred_element_type=jnp.float32
    ).astype(jnp.bfloat16)
    outgoing = own_spectra.reshape(own_spectra.shape[:3] + (2, freqs))[slot_for]
    arrived = lax.all_to_all(outgoing, "target", split_axis=0, concat_axis=0, tiled=True)
    data_real = jnp.moveaxis(data_spectra[0, :, 0], -1, 0)
    data_imag = jnp.moveaxis(data_spectra[0, :, 1], -1, 0)
    forward = jnp.stack(
        [jnp.stack([data_real, data_imag], 3), jnp.stack([-data_imag, data_real], 3)], 3
    )
    backward = jnp.stack(
        [jnp.stack([-data_real, -data_imag], 3), jnp.stack([data_imag, -data_real], 3)], 3
    )
    spectra = arrived[own_owner]
    partial_value = jnp.einsum(
        "lakcf,flkcdr->fdar", spectra, forward, preferred_element_type=jnp.float32
    )
    f_dim, parts, shots, recvs = partial_value.shape
    split_value = partial_value.reshape(f_dim, parts, shots, channels, recvs // channels)
    exchanged = lax.all_to_all(split_value, "surface", split_axis=3, concat_axis=3, tiled=True)
    summed_share = jnp.moveaxis(jnp.sum(exchanged, axis=3), 0, -1)
    residual_share = observed[0].astype(jnp.float32) - summed_share
    misfit_share = jnp.moveaxis(residual_share.astype(jnp.bfloat16), -1, 0)
    spread = jnp.broadcast_to(misfit_share[:, :, :, None], misfit_share.shape[:3] + (channels,) + misfit_share.shape[3:])
    gathered = lax.all_to_all(spread, "surface", split_axis=3, concat_axis=3, tiled=True)
    misfit = gathered.reshape(f_dim, parts, shots, recvs)
    match = own_owner[None, :] == jnp.arange(owners, dtype=jnp.int32)[:, None]
    entry_for = jnp.argmax(match, axis=1)
    positions = response.shape[2]
    width = positions // chunks
    next_parts = []
    for c in range(chunks):
        lo, hi = c * width, (c + 1) * width
        grad_spectra = jnp.einsum(
            "fcar,flkecr->lakef", misfit, backward[:, :, lo:hi], preferred_element_type=jnp.float32
        )
        grad_flat = grad_spectra.reshape(grad_spectra.shape[:3] + (samples,))
        grad_time = jnp.dot(grad_flat, dft_table.T, precision=lax.Precision.HIGH)
        returning = grad_time.astype(jnp.bfloat16)[entry_for]
        received = lax.all_to_all(returning, "target", split_axis=0, concat_axis=0, tiled=True)
        taken = jnp.where(
            chosen[:, :, None, None, None], received[None].astype(jnp.float32), jnp.zeros((), jnp.float32)
        )
        gradient = jnp.sum(taken, axis=1)
        next_parts.append(response[:, :, lo:hi] - step_length * gradient)
    response_next = next_parts[0] if chunks == 1 else jnp.concatenate(next_parts, axis=2)
    return (response_next, response_next.astype(jnp.bfloat16), residual_share[None])


def solution(mesh):
    return jax.shard_map(
        per_device,
        mesh=mesh,
        in_specs=(
            P("target", None, "surface", None),
            P("target", None, None, "surface", None, None),
            P("target", None, None, "surface", None),
            P(),
        ),
        out_specs=(
            P("target", None, "surface", None),
            P("target", None, "surface", None),
            P("target", None, None, "surface", None),
        ),
        check_vma=False,
    )
```

```python
import math

import jax
import jax.numpy as jnp
from jax import lax
from jax.sharding import PartitionSpec as P

step_length = 0.5
chunks = 2


def make_table(samples):
    freqs = samples // 2
    sample_index = lax.broadcasted_iota(jnp.int32, (samples, freqs), 0)
    freq_index = lax.broadcasted_iota(jnp.int32, (samples, freqs), 1)
    phase = (sample_index * freq_index % samples).astype(jnp.float32) * (2.0 * math.pi / samples)
    return jnp.concatenate([jnp.cos(phase), -jnp.sin(phase)], axis=1)


def contract(spec, listed):
    return jnp.einsum("lakf,lkrf->arf", spec, listed, preferred_element_type=jnp.float32)


def correlate(misfit_part, listed):
    return jnp.einsum("arf,lkrf->lakf", misfit_part, listed, preferred_element_type=jnp.float32)


def per_device(response, data_spectra, observed, block_lists):
    owners = lax.axis_size("target")
    channels = lax.axis_size("surface")
    my_index = lax.axis_index("target")
    owned = response.shape[0]
    samples = response.shape[3]
    freqs = samples // 2
    dft_table = make_table(samples)
    own_ids = lax.dynamic_slice_in_dim(block_lists, my_index, 1, 0)[0]
    own_owner = own_ids // owned
    wanted = block_lists // owned == my_index
    present = jnp.any(wanted, axis=1)
    slot_for = jnp.sum(jnp.where(wanted, block_lists % owned, 0), axis=1)
    chosen = (slot_for[None, :] == jnp.arange(owned, dtype=jnp.int32)[:, None]) & present[None, :]
    copy_now = response.astype(jnp.bfloat16)
    own_spectra = jnp.dot(
        copy_now, dft_table.astype(jnp.bfloat16), preferred_element_type=jnp.float32
    ).astype(jnp.bfloat16)
    outgoing = own_spectra.reshape(own_spectra.shape[:3] + (2, freqs))[slot_for]
    arrived = lax.all_to_all(outgoing, "target", split_axis=0, concat_axis=0, tiled=True)
    data_real = jnp.moveaxis(data_spectra[0, :, 0], -1, 0)
    data_imag = jnp.moveaxis(data_spectra[0, :, 1], -1, 0)
    forward = jnp.stack(
        [jnp.stack([data_real, data_imag], 3), jnp.stack([-data_imag, data_real], 3)], 3
    )
    backward = jnp.stack(
        [jnp.stack([-data_real, -data_imag], 3), jnp.stack([data_imag, -data_real], 3)], 3
    )
    spectra = arrived[own_owner]
    partial_value = jnp.einsum(
        "lakcf,flkcdr->fdar", spectra, forward, preferred_element_type=jnp.float32
    )
    f_dim, parts, shots, recvs = partial_value.shape
    split_value = partial_value.reshape(f_dim, parts, shots, channels, recvs // channels)
    exchanged = lax.all_to_all(split_value, "surface", split_axis=3, concat_axis=3, tiled=True)
    summed_share = jnp.moveaxis(jnp.sum(exchanged, axis=3), 0, -1)
    residual_share = observed[0].astype(jnp.float32) - summed_share
    misfit_share = jnp.moveaxis(residual_share.astype(jnp.bfloat16), -1, 0)
    spread = jnp.broadcast_to(misfit_share[:, :, :, None], misfit_share.shape[:3] + (channels,) + misfit_share.shape[3:])
    gathered = lax.all_to_all(spread, "surface", split_axis=3, concat_axis=3, tiled=True)
    misfit = gathered.reshape(f_dim, parts, shots, recvs)
    match = own_owner[None, :] == jnp.arange(owners, dtype=jnp.int32)[:, None]
    entry_for = jnp.argmax(match, axis=1)
    positions = response.shape[2]
    width = positions // chunks
    next_parts = []
    for c in range(chunks):
        lo, hi = c * width, (c + 1) * width
        grad_spectra = jnp.einsum(
            "fcar,flkecr->lakef", misfit, backward[:, :, lo:hi], preferred_element_type=jnp.float32
        )
        returning = grad_spectra.astype(jnp.bfloat16)[entry_for]
        received = lax.all_to_all(returning, "target", split_axis=0, concat_axis=0, tiled=True)
        taken = jnp.where(
            chosen[:, :, None, None, None, None], received[None].astype(jnp.float32), jnp.zeros((), jnp.float32)
        )
        summed = jnp.sum(taken, axis=1)
        summed_flat = summed.reshape(summed.shape[:3] + (samples,))
        gradient = jnp.dot(summed_flat, dft_table.T, precision=lax.Precision.HIGH)
        next_parts.append(response[:, :, lo:hi] - step_length * gradient)
    response_next = next_parts[0] if chunks == 1 else jnp.concatenate(next_parts, axis=2)
    return (response_next, response_next.astype(jnp.bfloat16), residual_share[None])


def solution(mesh):
    return jax.shard_map(
        per_device,
        mesh=mesh,
        in_specs=(
            P("target", None, "surface", None),
            P("target", None, None, "surface", None, None),
            P("target", None, None, "surface", None),
            P(),
        ),
        out_specs=(
            P("target", None, "surface", None),
            P("target", None, "surface", None),
            P("target", None, None, "surface", None),
        ),
        check_vma=False,
    )
```

```python
import math

import jax
import jax.numpy as jnp
from jax import lax
from jax.sharding import PartitionSpec as P

step_length = 0.5
chunks = 1


def make_table(samples):
    freqs = samples // 2
    sample_index = lax.broadcasted_iota(jnp.int32, (samples, freqs), 0)
    freq_index = lax.broadcasted_iota(jnp.int32, (samples, freqs), 1)
    phase = (sample_index * freq_index % samples).astype(jnp.float32) * (2.0 * math.pi / samples)
    return jnp.concatenate([jnp.cos(phase), -jnp.sin(phase)], axis=1)


def contract(spec, listed):
    return jnp.einsum("lakf,lkrf->arf", spec, listed, preferred_element_type=jnp.float32)


def correlate(misfit_part, listed):
    return jnp.einsum("arf,lkrf->lakf", misfit_part, listed, preferred_element_type=jnp.float32)


def per_device(response, data_spectra, observed, block_lists):
    owners = lax.axis_size("target")
    channels = lax.axis_size("surface")
    my_index = lax.axis_index("target")
    owned = response.shape[0]
    samples = response.shape[3]
    freqs = samples // 2
    dft_table = make_table(samples)
    own_ids = lax.dynamic_slice_in_dim(block_lists, my_index, 1, 0)[0]
    own_owner = own_ids // owned
    wanted = block_lists // owned == my_index
    present = jnp.any(wanted, axis=1)
    slot_for = jnp.sum(jnp.where(wanted, block_lists % owned, 0), axis=1)
    chosen = (slot_for[None, :] == jnp.arange(owned, dtype=jnp.int32)[:, None]) & present[None, :]
    copy_now = response.astype(jnp.bfloat16)
    own_spectra = jnp.dot(
        copy_now, dft_table.astype(jnp.bfloat16), preferred_element_type=jnp.float32
    ).astype(jnp.bfloat16)
    outgoing = own_spectra.reshape(own_spectra.shape[:3] + (2, freqs))[slot_for]
    arrived = lax.all_to_all(outgoing, "target", split_axis=0, concat_axis=0, tiled=True)
    data_real = jnp.moveaxis(data_spectra[0, :, 0], -1, 0)
    data_imag = jnp.moveaxis(data_spectra[0, :, 1], -1, 0)
    forward = jnp.stack(
        [jnp.stack([data_real, data_imag], 3), jnp.stack([-data_imag, data_real], 3)], 3
    )
    backward = jnp.stack(
        [jnp.stack([-data_real, -data_imag], 3), jnp.stack([data_imag, -data_real], 3)], 3
    )
    spectra = arrived[own_owner]
    partial_value = jnp.einsum(
        "lakcf,flkcdr->fdar", spectra, forward, preferred_element_type=jnp.float32
    )
    f_dim, parts, shots, recvs = partial_value.shape
    split_value = partial_value.reshape(f_dim, parts, shots, channels, recvs // channels)
    exchanged = lax.all_to_all(split_value, "surface", split_axis=3, concat_axis=3, tiled=True)
    summed_share = jnp.moveaxis(jnp.sum(exchanged, axis=3), 0, -1)
    residual_share = observed[0].astype(jnp.float32) - summed_share
    misfit_share = jnp.moveaxis(residual_share.astype(jnp.bfloat16), -1, 0)
    spread = jnp.broadcast_to(misfit_share[:, :, :, None], misfit_share.shape[:3] + (channels,) + misfit_share.shape[3:])
    gathered = lax.all_to_all(spread, "surface", split_axis=3, concat_axis=3, tiled=True)
    misfit = gathered.reshape(f_dim, parts, shots, recvs)
    match = own_owner[None, :] == jnp.arange(owners, dtype=jnp.int32)[:, None]
    entry_for = jnp.argmax(match, axis=1)
    positions = response.shape[2]
    width = positions // chunks
    next_parts = []
    for c in range(chunks):
        lo, hi = c * width, (c + 1) * width
        grad_spectra = jnp.einsum(
            "fcar,flkecr->lakef", misfit, backward[:, :, lo:hi], preferred_element_type=jnp.float32
        )
        returning = grad_spectra.astype(jnp.bfloat16)[entry_for]
        received = lax.all_to_all(returning, "target", split_axis=0, concat_axis=0, tiled=True)
        taken = jnp.where(
            chosen[:, :, None, None, None, None], received[None].astype(jnp.float32), jnp.zeros((), jnp.float32)
        )
        summed = jnp.sum(taken, axis=1)
        summed_flat = summed.reshape(summed.shape[:3] + (samples,))
        gradient = jnp.dot(summed_flat, dft_table.T, precision=lax.Precision.HIGH)
        next_parts.append(response[:, :, lo:hi] - step_length * gradient)
    response_next = next_parts[0] if chunks == 1 else jnp.concatenate(next_parts, axis=2)
    return (response_next, response_next.astype(jnp.bfloat16), residual_share[None])


def solution(mesh):
    return jax.shard_map(
        per_device,
        mesh=mesh,
        in_specs=(
            P("target", None, "surface", None),
            P("target", None, None, "surface", None, None),
            P("target", None, None, "surface", None),
            P(),
        ),
        out_specs=(
            P("target", None, "surface", None),
            P("target", None, "surface", None),
            P("target", None, None, "surface", None),
        ),
        check_vma=False,
    )
```
